512 devices in a mesh: heads: 8 (over y), ctx: 64 (over z, x, core).
Axes of the slice: x: 4, y: 8, z: 8, core: 2. Of those that a mesh axis runs over, the one named last changes fastest.
Arguments:
- queries: bfloat16 [16384, 4096], P('ctx', 'heads'), may hold values from -6 to 6
- keys: bfloat16 [16384, 1024], P('ctx', 'heads'), may hold values from -6 to 6
- values: bfloat16 [16384, 1024], P('ctx', 'heads'), may hold values from -6 to 6
- out_weight: bfloat16 [4096, 4096], P('heads'), may hold values from -0.09375 to 0.09375
- out_grad: bfloat16 [4096, 16384], P('heads', 'ctx'), may hold values from -6 to 6
- doc_lengths: int32 [16], replicated, may hold values from 1 to 1792, 16384 in all
Outputs:
- out_t: bfloat16 [4096, 16384], P('heads', 'ctx')
- grad_q: bfloat16 [16384, 4096], P('ctx', 'heads')
- grad_k: bfloat16 [16384, 1024], P('ctx', 'heads')
- grad_v: bfloat16 [16384, 1024], P('ctx', 'heads')
The draws below stay inside these ranges and needn't reach their ends.
Inputs may be any that keep to these rules, and one draw needn't show every extreme that they name: `doc_lengths`: the 16 lengths sum to 16384; the longest document has exactly 1792 tokens.
All inputs are finite; a program needn't handle non-finite values.
Results may differ from the reference program's by a relative error of at most 0.02.
Values may be sent and summed in bfloat16 or wider, within the bound.
No kernel may reach another device: no remote copies, remote signals or barrier semaphores. Data moves between devices by JAX's collectives and lax.ppermute only.
A program may use at most 64 MiB of HBM per device.

```python
import math
import jax
import jax.numpy as jnp
import numpy as np
from jax import lax

TOK_DEV = 256
D = 4096
HD = 128
REACH = 7
KVH = 8
HQ = 32
TOKENS = 16384
MAXDOC = 1792
NDOCS = 16
N_CTX = 64


def draw_queries(key, part):
    result = jax.random.truncated_normal(jax.random.fold_in(key, 1), -4.0, 4.0, (TOKENS, HQ * HD), jnp.float32)
    return result.astype(jnp.bfloat16)


def draw_keys(key, part):
    result = jax.random.truncated_normal(jax.random.fold_in(key, 2), -4.0, 4.0, (TOKENS, KVH * HD), jnp.float32)
    return result.astype(jnp.bfloat16)


def block_levels(key, extent, shards, smallest, high):
    loudness, own = 1.0, jax.random.fold_in(key, 6)
    for dim, shards_of in shards:
        steps = jnp.exp(jax.random.uniform(jax.random.fold_in(own, dim), (shards_of,), jnp.float32, smallest / len(shards), high / len(shards)))
        loudness = loudness * jnp.repeat(steps, extent[dim] // shards_of).reshape([-1 if axis == dim else 1 for axis in range(len(extent))])
    return loudness


def length_profile(number_of, total, limit, lean):
    portions = [(1 << 20) // math.isqrt(rank ** lean) + 1 for rank in range(2, number_of + 1)]
    spare, counts = total - limit - (number_of - 1), [1] * (number_of - 1)
    while spare > 0:
        free = [i for i in range(number_of - 1) if counts[i] < limit]
        pool, budget = sum([portions[i] for i in free]), spare
        for i in free:
            extra = min(limit - counts[i], max(1, budget * portions[i] // pool), spare)
            counts[i] = counts[i] + extra
            spare = spare - extra
    return np.array([limit] + counts)


def uneven(key, number_of, total, reach, lean):
    if number_of == 2:
        one = jax.random.randint(key, (), max(1, total - reach), min(reach, total - 1) + 1)
        return jnp.stack([one, total - one])
    tallies = jnp.asarray(length_profile(number_of, total, reach, lean), jnp.int32)
    twos = (number_of - 1) // 2
    donor, sink = tallies[1:1 + 2 * twos:2], tallies[2:2 + 2 * twos:2]
    slack = jnp.minimum(donor - 1, reach - sink)
    shifted = jax.random.randint(jax.random.fold_in(key, 1), (twos,), 0, 1 << 20) % (slack + 1)
    tallies = tallies.at[1:1 + 2 * twos:2].set(donor - shifted).at[2:2 + 2 * twos:2].set(sink + shifted)
    return tallies[jax.random.permutation(jax.random.fold_in(key, 2), number_of)]


def bell_draw(own_key, shape, deviation, limit, split=(), kind=jnp.bfloat16):
    entries = deviation * jax.random.normal(own_key, shape, jnp.float32)
    if split:
        entries = entries * block_levels(own_key, shape, split, -0.22, 0.18)
    return jnp.clip(entries, -limit, limit).astype(kind)


def setup_inputs(seed: int = 0) -> dict:
    key_of = jax.random.split(jax.random.key(seed), 7)
    return {
        "queries": draw_queries(jax.random.fold_in(key_of[6], 71), 0),
        "keys": draw_keys(jax.random.fold_in(key_of[6], 71), 0),
        "values": bell_draw(key_of[2], (TOKENS, KVH * HD), 1.0, 6.0, ((0, 64), (1, 8))),
        "out_weight": bell_draw(key_of[3], (HQ * HD, D), (HQ * HD) ** -0.5, 0.09375, ((0, 8),)),
        "out_grad": bell_draw(key_of[4], (D, TOKENS), 1.0, 6.0, ((0, 8), (1, 64))),
        "doc_lengths": uneven(key_of[5], NDOCS, TOKENS, MAXDOC, 2).astype(jnp.int32),
    }


def reference(queries, keys, values, out_weight, out_grad, doc_lengths):
    group_size = HQ // KVH
    padding = REACH * TOK_DEV
    window_len = padding + TOK_DEV
    scaling = 1.0 / math.sqrt(HD)
    doc_ends = jnp.cumsum(doc_lengths).astype(jnp.int32)
    starts = (doc_ends - doc_lengths).astype(jnp.int32)
    positions = jnp.arange(TOKENS, dtype=jnp.int32)
    first_key = lax.optimization_barrier(jnp.max(jnp.where(starts[None, :] <= positions[:, None], starts[None, :], 0), axis=1)).astype(jnp.int32)
    key_pad = jnp.concatenate([jnp.zeros((padding, KVH * HD), keys.dtype), keys], axis=0)
    value_pad = jnp.concatenate([jnp.zeros((padding, KVH * HD), values.dtype), values], axis=0)
    grad_attn = jnp.dot(out_weight, out_grad, preferred_element_type=jnp.float32).astype(jnp.bfloat16)

    def one_block(carry, block):
        grad_keys, grad_values = carry
        begin = (block * TOK_DEV).astype(jnp.int32)
        query_rows = lax.dynamic_slice_in_dim(queries, begin, TOK_DEV, 0).astype(jnp.float32).reshape(TOK_DEV, KVH, group_size, HD)
        key_rows = lax.dynamic_slice_in_dim(key_pad, begin, window_len, 0).astype(jnp.float32).reshape(window_len, KVH, HD)
        value_rows = lax.dynamic_slice_in_dim(value_pad, begin, window_len, 0).astype(jnp.float32).reshape(window_len, KVH, HD)
        grad_rows = lax.dynamic_slice_in_dim(grad_attn, begin, TOK_DEV, 1).astype(jnp.float32).reshape(KVH, group_size, HD, TOK_DEV)
        query_pos = begin + jnp.arange(TOK_DEV, dtype=jnp.int32)
        key_pos = begin - padding + jnp.arange(window_len, dtype=jnp.int32)
        lowest = lax.dynamic_slice_in_dim(first_key, begin, TOK_DEV, 0)
        visible = (key_pos[None, :] >= lowest[:, None]) & (key_pos[None, :] <= query_pos[:, None])
        scores = jnp.einsum('thgd,khd->hgtk', query_rows, key_rows) * scaling
        scores = jnp.where(visible[None, None], scores, -jnp.inf)
        largest = lax.optimization_barrier(jnp.max(scores, axis=-1, keepdims=True))
        expons = jnp.exp(scores - largest)
        weights = expons / lax.optimization_barrier(jnp.sum(expons, axis=-1, keepdims=True))
        probs = lax.optimization_barrier(weights.astype(jnp.bfloat16)).astype(jnp.float32)
        attn = jnp.einsum('hgtk,khd->thgd', probs, value_rows).astype(jnp.bfloat16)
        attn_float = lax.optimization_barrier(attn).astype(jnp.float32)
        delta_sum = jnp.einsum('thgd,hgdt->hgt', attn_float, grad_rows)
        grad_probs = jnp.einsum('hgdt,khd->hgtk', grad_rows, value_rows)
        dscore = (weights * (grad_probs - delta_sum[..., None]) * scaling).astype(jnp.bfloat16)
        dscore_float = lax.optimization_barrier(dscore).astype(jnp.float32)
        grad_query = jnp.einsum('hgtk,khd->thgd', dscore_float, key_rows).astype(jnp.bfloat16).reshape(TOK_DEV, HQ * HD)
        key_part = jnp.einsum('hgtk,thgd->khd', dscore_float, query_rows).reshape(window_len, KVH * HD)
        value_part = jnp.einsum('hgtk,hgdt->khd', probs, grad_rows).reshape(window_len, KVH * HD)
        grad_keys = lax.dynamic_update_slice_in_dim(grad_keys, lax.dynamic_slice_in_dim(grad_keys, begin, window_len, 0) + key_part, begin, 0)
        grad_values = lax.dynamic_update_slice_in_dim(grad_values, lax.dynamic_slice_in_dim(grad_values, begin, window_len, 0) + value_part, begin, 0)
        return ((grad_keys, grad_values), (attn.reshape(TOK_DEV, HQ * HD), grad_query))
    zero_acc = jnp.zeros((TOKENS + padding, KVH * HD), jnp.float32)
    (grad_keys, grad_values), (attn_rows, grad_query) = lax.scan(one_block, (zero_acc, zero_acc), jnp.arange(N_CTX, dtype=jnp.int32))
    attn_all = attn_rows.reshape(TOKENS, HQ * HD)
    out_t = jnp.dot(attn_all, out_weight, preferred_element_type=jnp.float32).astype(jnp.bfloat16).T
    grad_q = grad_query.reshape(TOKENS, HQ * HD)
    grad_k = grad_keys[padding:].astype(jnp.bfloat16)
    grad_v = grad_values[padding:].astype(jnp.bfloat16)
    return (out_t, grad_q, grad_k, grad_v)
```

```python
import math

import jax
import jax.numpy as jnp
from jax import lax
from jax.sharding import PartitionSpec as P

REACH = 7


def passed_along(value, axis, steps):
    count = lax.axis_size(axis)
    first, last = (max(0, -steps), min(count, count - steps))
    return lax.ppermute(value, axis, [(source, source + steps) for source in range(first, last)])


def per_device(queries, keys, values, out_weight, out_grad, doc_lengths):
    tok_rows = queries.shape[0]
    head_dim = keys.shape[1]
    group_size = queries.shape[1] // head_dim
    scaling = 1.0 / math.sqrt(head_dim)
    shard = lax.axis_index("ctx")
    doc_ends = jnp.cumsum(doc_lengths)
    starts = doc_ends - doc_lengths
    positions = shard * tok_rows + jnp.arange(tok_rows, dtype=jnp.int32)
    first_key = jnp.max(
        jnp.where(starts[None, :] <= positions[:, None], starts[None, :], 0), axis=1
    )
    stacked = jnp.concatenate([keys, values], axis=1)
    blocks = [stacked[None]]
    for offset in range(1, REACH + 1):
        blocks.append(passed_along(stacked, "ctx", offset)[None])
    window = jnp.concatenate(blocks, axis=0)
    num_blocks = window.shape[0]
    flat_keys = window[:, :, :head_dim].reshape(num_blocks * tok_rows, head_dim)
    flat_values = window[:, :, head_dim:].reshape(num_blocks * tok_rows, head_dim)
    key_pos = (
        (shard - jnp.arange(num_blocks, dtype=jnp.int32))[:, None] * tok_rows
        + jnp.arange(tok_rows, dtype=jnp.int32)[None, :]
    ).reshape(-1)
    visible = (key_pos[None, :] >= first_key[:, None]) & (key_pos[None, :] <= positions[:, None])
    query_heads = queries.reshape(tok_rows, group_size, head_dim)
    scores = (
        jnp.einsum("tgd,kd->gtk", query_heads, flat_keys, preferred_element_type=jnp.float32)
        * scaling
    )
    scores = jnp.where(visible[None], scores, -jnp.inf)
    largest = jnp.max(scores, axis=-1, keepdims=True)
    expons = jnp.exp(scores - largest)
    weights = expons / jnp.sum(expons, axis=-1, keepdims=True)
    probs = weights.astype(jnp.bfloat16)
    attn_heads = jnp.einsum(
        "gtk,kd->tgd", probs, flat_values, preferred_element_type=jnp.float32
    ).astype(jnp.bfloat16)
    attn = attn_heads.reshape(tok_rows, group_size * head_dim)
    out_partial = lax.dot_general(
        out_weight, attn, (((0,), (1,)), ((), ())), preferred_element_type=jnp.float32
    ).astype(jnp.bfloat16)
    gathered = lax.all_gather(out_grad, "heads", axis=0, tiled=True)
    out_t = lax.psum_scatter(
        out_partial, "heads", scatter_dimension=0, tiled=True
    )
    _, gathered = lax.optimization_barrier((out_partial, gathered))
    grad_attn = jnp.dot(
        out_weight,
        gathered,
        preferred_element_type=jnp.float32,
    ).astype(jnp.bfloat16)
    grad_heads = grad_attn.reshape(group_size, head_dim, tok_rows)
    delta_sum = jnp.einsum(
        "tgd,gdt->gt", attn_heads, grad_heads, preferred_element_type=jnp.float32
    )
    grad_probs = jnp.einsum(
        "gdt,kd->gtk", grad_heads, flat_values, preferred_element_type=jnp.float32
    )
    dscore = (weights * (grad_probs - delta_sum[:, :, None]) * scaling).astype(jnp.bfloat16)
    grad_q = (
        jnp.einsum("gtk,kd->tgd", dscore, flat_keys, preferred_element_type=jnp.float32)
        .astype(jnp.bfloat16)
        .reshape(tok_rows, group_size * head_dim)
    )
    key_part = jnp.einsum("gtk,tgd->kd", dscore, query_heads, preferred_element_type=jnp.float32)
    value_part = jnp.einsum("gtk,gdt->kd", probs, grad_heads, preferred_element_type=jnp.float32)
    partial_grads = jnp.concatenate([key_part, value_part], axis=1).reshape(
        num_blocks, tok_rows, 2 * head_dim
    )
    summed = partial_grads[0]
    for offset in range(1, num_blocks):
        sent = passed_along(partial_grads[offset].astype(jnp.bfloat16), "ctx", -offset)
        summed = summed + sent.astype(jnp.float32)
    grad_k = summed[:, :head_dim].astype(jnp.bfloat16)
    grad_v = summed[:, head_dim:].astype(jnp.bfloat16)
    return (out_t, grad_q, grad_k, grad_v)


def solution(mesh):
    placed = (
        P("ctx", "heads"),
        P("ctx", "heads"),
        P("ctx", "heads"),
        P("heads", None),
        P("heads", "ctx"),
        P(),
    )
    return jax.shard_map(
        per_device,
        mesh=mesh,
        in_specs=placed,
        out_specs=(P("heads", "ctx"), P("ctx", "heads"), P("ctx", "heads"), P("ctx", "heads")),
        check_vma=False,
    )
```

```python
import math

import jax
import jax.numpy as jnp
from jax import lax
from jax.sharding import PartitionSpec as P

REACH = 7


def passed_along(value, axis, steps):
    count = lax.axis_size(axis)
    first, last = (max(0, -steps), min(count, count - steps))
    return lax.ppermute(value, axis, [(source, source + steps) for source in range(first, last)])


def ring_shift(value, axis, steps):
    count = lax.axis_size(axis)
    return lax.ppermute(value, axis, [(source, (source + steps) % count) for source in range(count)])


def weight_columns(out_weight, index, begin, width):
    block = out_weight.shape[0]
    return lax.dynamic_slice_in_dim(out_weight, index * block + begin, width, axis=1)


def ring_gather_dot(out_weight, out_grad, axis):
    count = lax.axis_size(axis)
    me = lax.axis_index(axis)
    block = out_grad.shape[0]
    half = block // 2

    def term(index, begin, width, piece):
        return jnp.dot(
            weight_columns(out_weight, index % count, begin, width),
            piece,
            preferred_element_type=jnp.float32,
        )

    total = term(me, 0, block, out_grad)
    ahead, behind = out_grad, out_grad
    for step in range(1, count // 2 + 1):
        if step < count - step:
            ahead = ring_shift(ahead, axis, 1)
            behind = ring_shift(behind, axis, -1)
            total = total + term(me - step, 0, block, ahead)
            total = total + term(me + step, 0, block, behind)
        else:
            low = ring_shift(ahead[:half], axis, 1)
            high = ring_shift(behind[half:], axis, -1)
            total = total + term(me - step, 0, half, low)
            total = total + term(me - step, half, half, high)
    return total


def ring_reduce_scatter_out(out_weight, attn, axis):
    count = lax.axis_size(axis)
    me = lax.axis_index(axis)
    block = out_weight.shape[0]
    half = block // 2

    def term(index, begin):
        return lax.dot_general(
            weight_columns(out_weight, index % count, begin, half),
            attn,
            (((0,), (1,)), ((), ())),
            preferred_element_type=jnp.float32,
        )

    low = term(me - 1, 0)
    high = term(me + 1, half)
    for step in range(1, count):
        low = ring_shift(low.astype(jnp.bfloat16), axis, 1).astype(jnp.float32) + term(me - 1 - step, 0)
        high = ring_shift(high.astype(jnp.bfloat16), axis, -1).astype(jnp.float32) + term(
            me + 1 + step, half
        )
    return jnp.concatenate([low, high], axis=0).astype(jnp.bfloat16)


def per_device(queries, keys, values, out_weight, out_grad, doc_lengths):
    tok_rows = queries.shape[0]
    head_dim = keys.shape[1]
    group_size = queries.shape[1] // head_dim
    scaling = 1.0 / math.sqrt(head_dim)
    shard = lax.axis_index("ctx")
    doc_ends = jnp.cumsum(doc_lengths)
    starts = doc_ends - doc_lengths
    positions = shard * tok_rows + jnp.arange(tok_rows, dtype=jnp.int32)
    first_key = jnp.max(
        jnp.where(starts[None, :] <= positions[:, None], starts[None, :], 0), axis=1
    )
    stacked = jnp.concatenate([keys, values], axis=1)
    blocks = [stacked[None]]
    for offset in range(1, REACH + 1):
        blocks.append(passed_along(stacked, "ctx", offset)[None])
    window = jnp.concatenate(blocks, axis=0)
    num_blocks = window.shape[0]
    flat_keys = window[:, :, :head_dim].reshape(num_blocks * tok_rows, head_dim)
    flat_values = window[:, :, head_dim:].reshape(num_blocks * tok_rows, head_dim)
    key_pos = (
        (shard - jnp.arange(num_blocks, dtype=jnp.int32))[:, None] * tok_rows
        + jnp.arange(tok_rows, dtype=jnp.int32)[None, :]
    ).reshape(-1)
    visible = (key_pos[None, :] >= first_key[:, None]) & (key_pos[None, :] <= positions[:, None])
    query_heads = queries.reshape(tok_rows, group_size, head_dim)
    scores = (
        jnp.einsum("tgd,kd->gtk", query_heads, flat_keys, preferred_element_type=jnp.float32)
        * scaling
    )
    scores = jnp.where(visible[None], scores, -jnp.inf)
    largest = jnp.max(scores, axis=-1, keepdims=True)
    expons = jnp.exp(scores - largest)
    weights = expons / jnp.sum(expons, axis=-1, keepdims=True)
    probs = weights.astype(jnp.bfloat16)
    attn_heads = jnp.einsum(
        "gtk,kd->tgd", probs, flat_values, preferred_element_type=jnp.float32
    ).astype(jnp.bfloat16)
    attn = attn_heads.reshape(tok_rows, group_size * head_dim)
    out_t = ring_reduce_scatter_out(out_weight, attn, "heads")
    grad_attn = ring_gather_dot(out_weight, out_grad, "heads").astype(jnp.bfloat16)
    grad_heads = grad_attn.reshape(group_size, head_dim, tok_rows)
    delta_sum = jnp.einsum(
        "tgd,gdt->gt", attn_heads, grad_heads, preferred_element_type=jnp.float32
    )
    grad_probs = jnp.einsum(
        "gdt,kd->gtk", grad_heads, flat_values, preferred_element_type=jnp.float32
    )
    dscore = (weights * (grad_probs - delta_sum[:, :, None]) * scaling).astype(jnp.bfloat16)
    grad_q = (
        jnp.einsum("gtk,kd->tgd", dscore, flat_keys, preferred_element_type=jnp.float32)
        .astype(jnp.bfloat16)
        .reshape(tok_rows, group_size * head_dim)
    )
    key_part = jnp.einsum("gtk,tgd->kd", dscore, query_heads, preferred_element_type=jnp.float32)
    value_part = jnp.einsum("gtk,gdt->kd", probs, grad_heads, preferred_element_type=jnp.float32)
    partial_grads = jnp.concatenate([key_part, value_part], axis=1).reshape(
        num_blocks, tok_rows, 2 * head_dim
    )
    summed = partial_grads[0]
    for offset in range(1, num_blocks):
        sent = passed_along(partial_grads[offset].astype(jnp.bfloat16), "ctx", -offset)
        summed = summed + sent.astype(jnp.float32)
    grad_k = summed[:, :head_dim].astype(jnp.bfloat16)
    grad_v = summed[:, head_dim:].astype(jnp.bfloat16)
    return (out_t, grad_q, grad_k, grad_v)


def solution(mesh):
    placed = (
        P("ctx", "heads"),
        P("ctx", "heads"),
        P("ctx", "heads"),
        P("heads", None),
        P("heads", "ctx"),
        P(),
    )
    return jax.shard_map(
        per_device,
        mesh=mesh,
        in_specs=placed,
        out_specs=(P("heads", "ctx"), P("ctx", "heads"), P("ctx", "heads"), P("ctx", "heads")),
        check_vma=False,
    )
```

```python
import math

import jax
import jax.numpy as jnp
from jax import lax
from jax.sharding import PartitionSpec as P

REACH = 7


def passed_along(value, axis, steps):
    count = lax.axis_size(axis)
    first, last = (max(0, -steps), min(count, count - steps))
    return lax.ppermute(value, axis, [(source, source + steps) for source in range(first, last)])


def per_device(queries, keys, values, out_weight, out_grad, doc_lengths):
    tok_rows = queries.shape[0]
    head_dim = keys.shape[1]
    group_size = queries.shape[1] // head_dim
    scaling = 1.0 / math.sqrt(head_dim)
    shard = lax.axis_index("ctx")
    doc_ends = jnp.cumsum(doc_lengths)
    starts = doc_ends - doc_lengths
    positions = shard * tok_rows + jnp.arange(tok_rows, dtype=jnp.int32)
    first_key = jnp.max(
        jnp.where(starts[None, :] <= positions[:, None], starts[None, :], 0), axis=1
    )
    stacked = jnp.concatenate([keys, values], axis=1)
    window = stacked[None]
    while window.shape[0] < REACH + 1:
        window = jnp.concatenate([window, passed_along(window, "ctx", window.shape[0])], axis=0)
    num_blocks = window.shape[0]
    flat_keys = window[:, :, :head_dim].reshape(num_blocks * tok_rows, head_dim)
    flat_values = window[:, :, head_dim:].reshape(num_blocks * tok_rows, head_dim)
    key_pos = (
        (shard - jnp.arange(num_blocks, dtype=jnp.int32))[:, None] * tok_rows
        + jnp.arange(tok_rows, dtype=jnp.int32)[None, :]
    ).reshape(-1)
    visible = (key_pos[None, :] >= first_key[:, None]) & (key_pos[None, :] <= positions[:, None])
    query_heads = queries.reshape(tok_rows, group_size, head_dim)
    scores = (
        jnp.einsum("tgd,kd->gtk", query_heads, flat_keys, preferred_element_type=jnp.float32)
        * scaling
    )
    scores = jnp.where(visible[None], scores, -jnp.inf)
    largest = jnp.max(scores, axis=-1, keepdims=True)
    expons = jnp.exp(scores - largest)
    weights = expons / jnp.sum(expons, axis=-1, keepdims=True)
    probs = weights.astype(jnp.bfloat16)
    attn_heads = jnp.einsum(
        "gtk,kd->tgd", probs, flat_values, preferred_element_type=jnp.float32
    ).astype(jnp.bfloat16)
    attn = attn_heads.reshape(tok_rows, group_size * head_dim)
    out_partial = lax.dot_general(
        out_weight, attn, (((0,), (1,)), ((), ())), preferred_element_type=jnp.float32
    ).astype(jnp.bfloat16)
    gathered = lax.all_gather(out_grad, "heads", axis=0, tiled=True)
    out_t = lax.psum_scatter(
        out_partial, "heads", scatter_dimension=0, tiled=True
    )
    _, gathered = lax.optimization_barrier((out_partial, gathered))
    grad_attn = jnp.dot(
        out_weight,
        gathered,
        preferred_element_type=jnp.float32,
    ).astype(jnp.bfloat16)
    grad_heads = grad_attn.reshape(group_size, head_dim, tok_rows)
    delta_sum = jnp.einsum(
        "tgd,gdt->gt", attn_heads, grad_heads, preferred_element_type=jnp.float32
    )
    grad_probs = jnp.einsum(
        "gdt,kd->gtk", grad_heads, flat_values, preferred_element_type=jnp.float32
    )
    dscore = (weights * (grad_probs - delta_sum[:, :, None]) * scaling).astype(jnp.bfloat16)
    grad_q = (
        jnp.einsum("gtk,kd->tgd", dscore, flat_keys, preferred_element_type=jnp.float32)
        .astype(jnp.bfloat16)
        .reshape(tok_rows, group_size * head_dim)
    )
    key_part = jnp.einsum("gtk,tgd->kd", dscore, query_heads, preferred_element_type=jnp.float32)
    value_part = jnp.einsum("gtk,gdt->kd", probs, grad_heads, preferred_element_type=jnp.float32)
    partial_grads = jnp.concatenate([key_part, value_part], axis=1).reshape(
        num_blocks, tok_rows, 2 * head_dim
    )
    summed = partial_grads
    while summed.shape[0] > 1:
        half = summed.shape[0] // 2
        sent = passed_along(summed[half:].astype(jnp.bfloat16), "ctx", -half)
        summed = summed[:half] + sent.astype(jnp.float32)
    summed = summed[0]
    grad_k = summed[:, :head_dim].astype(jnp.bfloat16)
    grad_v = summed[:, head_dim:].astype(jnp.bfloat16)
    return (out_t, grad_q, grad_k, grad_v)


def solution(mesh):
    placed = (
        P("ctx", "heads"),
        P("ctx", "heads"),
        P("ctx", "heads"),
        P("heads", None),
        P("heads", "ctx"),
        P(),
    )
    return jax.shard_map(
        per_device,
        mesh=mesh,
        in_specs=placed,
        out_specs=(P("heads", "ctx"), P("ctx", "heads"), P("ctx", "heads"), P("ctx", "heads")),
        check_vma=False,
    )
```

```python
import math

import jax
import jax.numpy as jnp
from jax import lax
from jax.experimental.layout import Layout, with_layout_constraint
from jax.sharding import PartitionSpec as P

REACH = 7


def passed_along(value, axis, steps):
    count = lax.axis_size(axis)
    first, last = (max(0, -steps), min(count, count - steps))
    return lax.ppermute(value, axis, [(source, source + steps) for source in range(first, last)])


def per_device(queries, keys, values, out_weight, out_grad, doc_lengths):
    tok_rows = queries.shape[0]
    head_dim = keys.shape[1]
    group_size = queries.shape[1] // head_dim
    scaling = 1.0 / math.sqrt(head_dim)
    shard = lax.axis_index("ctx")
    doc_ends = jnp.cumsum(doc_lengths)
    starts = doc_ends - doc_lengths
    positions = shard * tok_rows + jnp.arange(tok_rows, dtype=jnp.int32)
    first_key = jnp.max(
        jnp.where(starts[None, :] <= positions[:, None], starts[None, :], 0), axis=1
    )
    stacked = jnp.concatenate([keys, values], axis=1)
    window = stacked[None]
    while window.shape[0] < REACH + 1:
        window = jnp.concatenate([window, passed_along(window, "ctx", window.shape[0])], axis=0)
    num_blocks = window.shape[0]
    flat_keys = window[:, :, :head_dim].reshape(num_blocks * tok_rows, head_dim)
    flat_values = window[:, :, head_dim:].reshape(num_blocks * tok_rows, head_dim)
    key_pos = (
        (shard - jnp.arange(num_blocks, dtype=jnp.int32))[:, None] * tok_rows
        + jnp.arange(tok_rows, dtype=jnp.int32)[None, :]
    ).reshape(-1)
    visible = (key_pos[None, :] >= first_key[:, None]) & (key_pos[None, :] <= positions[:, None])
    query_heads = queries.reshape(tok_rows, group_size, head_dim)
    scores = (
        jnp.einsum("tgd,kd->gtk", query_heads, flat_keys, preferred_element_type=jnp.float32)
        * scaling
    )
    scores = jnp.where(visible[None], scores, -jnp.inf)
    largest = jnp.max(scores, axis=-1, keepdims=True)
    expons = jnp.exp(scores - largest)
    weights = expons / jnp.sum(expons, axis=-1, keepdims=True)
    probs = weights.astype(jnp.bfloat16)
    attn_heads = jnp.einsum(
        "gtk,kd->tgd", probs, flat_values, preferred_element_type=jnp.float32
    ).astype(jnp.bfloat16)
    attn = attn_heads.reshape(tok_rows, group_size * head_dim)
    out_partial = lax.dot_general(
        out_weight, attn, (((0,), (1,)), ((), ())), preferred_element_type=jnp.float32
    ).astype(jnp.bfloat16)
    out_partial = with_layout_constraint(out_partial, Layout((0, 1)))
    gathered = lax.all_gather(out_grad, "heads", axis=0, tiled=True)
    out_t = lax.psum_scatter(
        out_partial, "heads", scatter_dimension=0, tiled=True
    )
    _, gathered = lax.optimization_barrier((out_partial, gathered))
    grad_attn = jnp.dot(
        out_weight,
        gathered,
        preferred_element_type=jnp.float32,
    ).astype(jnp.bfloat16)
    grad_heads = grad_attn.reshape(group_size, head_dim, tok_rows)
    delta_sum = jnp.einsum(
        "tgd,gdt->gt", attn_heads, grad_heads, preferred_element_type=jnp.float32
    )
    grad_probs = jnp.einsum(
        "gdt,kd->gtk", grad_heads, flat_values, preferred_element_type=jnp.float32
    )
    dscore = (weights * (grad_probs - delta_sum[:, :, None]) * scaling).astype(jnp.bfloat16)
    grad_q = (
        jnp.einsum("gtk,kd->tgd", dscore, flat_keys, preferred_element_type=jnp.float32)
        .astype(jnp.bfloat16)
        .reshape(tok_rows, group_size * head_dim)
    )
    key_part = jnp.einsum("gtk,tgd->kd", dscore, query_heads, preferred_element_type=jnp.float32)
    value_part = jnp.einsum("gtk,gdt->kd", probs, grad_heads, preferred_element_type=jnp.float32)
    partial_grads = jnp.concatenate([key_part, value_part], axis=1).reshape(
        num_blocks, tok_rows, 2 * head_dim
    )
    summed = partial_grads
    while summed.shape[0] > 1:
        half = summed.shape[0] // 2
        sent = passed_along(summed[half:].astype(jnp.bfloat16), "ctx", -half)
        summed = summed[:half] + sent.astype(jnp.float32)
    summed = summed[0]
    grad_k = summed[:, :head_dim].astype(jnp.bfloat16)
    grad_v = summed[:, head_dim:].astype(jnp.bfloat16)
    return (out_t, grad_q, grad_k, grad_v)


def solution(mesh):
    placed = (
        P("ctx", "heads"),
        P("ctx", "heads"),
        P("ctx", "heads"),
        P("heads", None),
        P("heads", "ctx"),
        P(),
    )
    return jax.shard_map(
        per_device,
        mesh=mesh,
        in_specs=placed,
        out_specs=(P("heads", "ctx"), P("ctx", "heads"), P("ctx", "heads"), P("ctx", "heads")),
        check_vma=False,
    )
```

```python
import math

import jax
import jax.numpy as jnp
from jax import lax
from jax.experimental.layout import Layout, with_layout_constraint
from jax.sharding import PartitionSpec as P

REACH = 7


def passed_along(value, axis, steps):
    count = lax.axis_size(axis)
    first, last = (max(0, -steps), min(count, count - steps))
    return lax.ppermute(value, axis, [(source, source + steps) for source in range(first, last)])


def per_device(queries, keys, values, out_weight, out_grad, doc_lengths):
    tok_rows = queries.shape[0]
    head_dim = keys.shape[1]
    group_size = queries.shape[1] // head_dim
    scaling = 1.0 / math.sqrt(head_dim)
    shard = lax.axis_index("ctx")
    doc_ends = jnp.cumsum(doc_lengths)
    starts = doc_ends - doc_lengths
    positions = shard * tok_rows + jnp.arange(tok_rows, dtype=jnp.int32)
    first_key = jnp.max(
        jnp.where(starts[None, :] <= positions[:, None], starts[None, :], 0), axis=1
    )
    stacked = jnp.concatenate([keys, values], axis=1)
    window = stacked[None]
    while window.shape[0] < REACH + 1:
        window = jnp.concatenate([window, passed_along(window, "ctx", window.shape[0])], axis=0)
    num_blocks = window.shape[0]
    flat_keys = window[:, :, :head_dim].reshape(num_blocks * tok_rows, head_dim)
    flat_values = window[:, :, head_dim:].reshape(num_blocks * tok_rows, head_dim)
    key_pos = (
        (shard - jnp.arange(num_blocks, dtype=jnp.int32))[:, None] * tok_rows
        + jnp.arange(tok_rows, dtype=jnp.int32)[None, :]
    ).reshape(-1)
    visible = (key_pos[None, :] >= first_key[:, None]) & (key_pos[None, :] <= positions[:, None])
    query_heads = queries.reshape(tok_rows, group_size, head_dim)
    scores = (
        jnp.einsum("tgd,kd->gtk", query_heads, flat_keys, preferred_element_type=jnp.float32)
        * scaling
    )
    scores = jnp.where(visible[None], scores, -jnp.inf)
    largest = jnp.max(scores, axis=-1, keepdims=True)
    expons = jnp.exp(scores - largest)
    weights = expons / jnp.sum(expons, axis=-1, keepdims=True)
    probs = weights.astype(jnp.bfloat16)
    attn_heads = jnp.einsum(
        "gtk,kd->tgd", probs, flat_values, preferred_element_type=jnp.float32
    ).astype(jnp.bfloat16)
    attn = attn_heads.reshape(tok_rows, group_size * head_dim)
    out_partial = lax.dot_general(
        out_weight, attn, (((0,), (1,)), ((), ())), preferred_element_type=jnp.float32
    ).astype(jnp.bfloat16)
    out_partial = with_layout_constraint(out_partial, Layout((0, 1)))
    gathered = lax.all_gather(out_grad, "heads", axis=0, tiled=True)
    out_t = lax.psum_scatter(
        out_partial, "heads", scatter_dimension=0, tiled=True
    )
    _, gathered = lax.optimization_barrier((out_partial, gathered))
    grad_attn = jnp.dot(
        out_weight,
        gathered,
        preferred_element_type=jnp.float32,
    ).astype(jnp.bfloat16)
    grad_heads = grad_attn.reshape(group_size, head_dim, tok_rows)
    delta_sum = jnp.einsum(
        "tgd,gdt->gt", attn_heads, grad_heads, preferred_element_type=jnp.float32
    )
    grad_probs = jnp.einsum(
        "gdt,kd->gtk", grad_heads, flat_values, preferred_element_type=jnp.float32
    )
    dscore = (weights * (grad_probs - delta_sum[:, :, None]) * scaling).astype(jnp.bfloat16)
    grad_q = (
        jnp.einsum("gtk,kd->tgd", dscore, flat_keys, preferred_element_type=jnp.float32)
        .astype(jnp.bfloat16)
        .reshape(tok_rows, group_size * head_dim)
    )
    key_part = jnp.einsum("gtk,tgd->kd", dscore, query_heads, preferred_element_type=jnp.float32)
    value_part = jnp.einsum("gtk,gdt->kd", probs, grad_heads, preferred_element_type=jnp.float32)
    partial_grads = jnp.concatenate([key_part, value_part], axis=1).reshape(
        num_blocks, tok_rows, 2 * head_dim
    )
    summed = partial_grads[0]
    for offset in range(1, num_blocks):
        sent = passed_along(partial_grads[offset].astype(jnp.bfloat16), "ctx", -offset)
        summed = summed + sent.astype(jnp.float32)
    grad_k = summed[:, :head_dim].astype(jnp.bfloat16)
    grad_v = summed[:, head_dim:].astype(jnp.bfloat16)
    return (out_t, grad_q, grad_k, grad_v)


def solution(mesh):
    placed = (
        P("ctx", "heads"),
        P("ctx", "heads"),
        P("ctx", "heads"),
        P("heads", None),
        P("heads", "ctx"),
        P(),
    )
    return jax.shard_map(
        per_device,
        mesh=mesh,
        in_specs=placed,
        out_specs=(P("heads", "ctx"), P("ctx", "heads"), P("ctx", "heads"), P("ctx", "heads")),
        check_vma=False,
    )
```

```python
import math

import jax
import jax.numpy as jnp
from jax import lax
from jax.experimental.layout import Layout, with_layout_constraint
from jax.sharding import PartitionSpec as P

REACH = 7


def passed_along(value, axis, steps):
    count = lax.axis_size(axis)
    first, last = (max(0, -steps), min(count, count - steps))
    return lax.ppermute(value, axis, [(source, source + steps) for source in range(first, last)])


def per_device(queries, keys, values, out_weight, out_grad, doc_lengths):
    tok_rows = queries.shape[0]
    head_dim = keys.shape[1]
    group_size = queries.shape[1] // head_dim
    scaling = 1.0 / math.sqrt(head_dim)
    shard = lax.axis_index("ctx")
    doc_ends = jnp.cumsum(doc_lengths)
    starts = doc_ends - doc_lengths
    positions = shard * tok_rows + jnp.arange(tok_rows, dtype=jnp.int32)
    first_key = jnp.max(
        jnp.where(starts[None, :] <= positions[:, None], starts[None, :], 0), axis=1
    )
    stacked = jnp.concatenate([keys, values], axis=1)
    window = stacked[None]
    while 2 * window.shape[0] < REACH + 1:
        window = jnp.concatenate([window, passed_along(window, "ctx", window.shape[0])], axis=0)
    reach = window.shape[0]
    key_window = window[:, :, :head_dim]
    value_window = window[:, :, head_dim:]
    key_window = jnp.concatenate([key_window, passed_along(key_window, "ctx", reach)], axis=0)
    value_sent = passed_along(value_window, "ctx", reach)
    num_blocks = key_window.shape[0]
    flat_keys = key_window.reshape(num_blocks * tok_rows, head_dim)
    key_pos = (
        (shard - jnp.arange(num_blocks, dtype=jnp.int32))[:, None] * tok_rows
        + jnp.arange(tok_rows, dtype=jnp.int32)[None, :]
    ).reshape(-1)
    visible = (key_pos[None, :] >= first_key[:, None]) & (key_pos[None, :] <= positions[:, None])
    query_heads = queries.reshape(tok_rows, group_size, head_dim)
    scores = (
        jnp.einsum("tgd,kd->gtk", query_heads, flat_keys, preferred_element_type=jnp.float32)
        * scaling
    )
    scores = jnp.where(visible[None], scores, -jnp.inf)
    largest = jnp.max(scores, axis=-1, keepdims=True)
    expons = jnp.exp(scores - largest)
    weights = expons / jnp.sum(expons, axis=-1, keepdims=True)
    value_sent, weights = lax.optimization_barrier((value_sent, weights))
    value_window = jnp.concatenate([value_window, value_sent], axis=0)
    flat_values = value_window.reshape(num_blocks * tok_rows, head_dim)
    probs = weights.astype(jnp.bfloat16)
    attn_heads = jnp.einsum(
        "gtk,kd->tgd", probs, flat_values, preferred_element_type=jnp.float32
    ).astype(jnp.bfloat16)
    attn = attn_heads.reshape(tok_rows, group_size * head_dim)
    out_partial = lax.dot_general(
        out_weight, attn, (((0,), (1,)), ((), ())), preferred_element_type=jnp.float32
    ).astype(jnp.bfloat16)
    out_partial = with_layout_constraint(out_partial, Layout((0, 1)))
    gathered = lax.all_gather(out_grad, "heads", axis=0, tiled=True)
    out_t = lax.psum_scatter(
        out_partial, "heads", scatter_dimension=0, tiled=True
    )
    _, gathered = lax.optimization_barrier((out_partial, gathered))
    grad_attn = jnp.dot(
        out_weight,
        gathered,
        preferred_element_type=jnp.float32,
    ).astype(jnp.bfloat16)
    grad_heads = grad_attn.reshape(group_size, head_dim, tok_rows)
    delta_sum = jnp.einsum(
        "tgd,gdt->gt", attn_heads, grad_heads, preferred_element_type=jnp.float32
    )
    grad_probs = jnp.einsum(
        "gdt,kd->gtk", grad_heads, flat_values, preferred_element_type=jnp.float32
    )
    dscore = (weights * (grad_probs - delta_sum[:, :, None]) * scaling).astype(jnp.bfloat16)
    grad_q = (
        jnp.einsum("gtk,kd->tgd", dscore, flat_keys, preferred_element_type=jnp.float32)
        .astype(jnp.bfloat16)
        .reshape(tok_rows, group_size * head_dim)
    )
    key_part = jnp.einsum("gtk,tgd->kd", dscore, query_heads, preferred_element_type=jnp.float32)
    value_part = jnp.einsum("gtk,gdt->kd", probs, grad_heads, preferred_element_type=jnp.float32)
    partial_grads = jnp.concatenate([key_part, value_part], axis=1).reshape(
        num_blocks, tok_rows, 2 * head_dim
    )
    summed = partial_grads[0]
    for offset in range(1, num_blocks):
        sent = passed_along(partial_grads[offset].astype(jnp.bfloat16), "ctx", -offset)
        summed = summed + sent.astype(jnp.float32)
    grad_k = summed[:, :head_dim].astype(jnp.bfloat16)
    grad_v = summed[:, head_dim:].astype(jnp.bfloat16)
    return (out_t, grad_q, grad_k, grad_v)


def solution(mesh):
    placed = (
        P("ctx", "heads"),
        P("ctx", "heads"),
        P("ctx", "heads"),
        P("heads", None),
        P("heads", "ctx"),
        P(),
    )
    return jax.shard_map(
        per_device,
        mesh=mesh,
        in_specs=placed,
        out_specs=(P("heads", "ctx"), P("ctx", "heads"), P("ctx", "heads"), P("ctx", "heads")),
        check_vma=False,
    )
```

```python
import math

import jax
import jax.numpy as jnp
from jax import lax
from jax.experimental.layout import Layout, with_layout_constraint
from jax.sharding import PartitionSpec as P

REACH = 7


def passed_along(value, axis, steps):
    count = lax.axis_size(axis)
    first, last = (max(0, -steps), min(count, count - steps))
    return lax.ppermute(value, axis, [(source, source + steps) for source in range(first, last)])


def ring_shift(value, axis, steps):
    count = lax.axis_size(axis)
    return lax.ppermute(value, axis, [(source, (source + steps) % count) for source in range(count)])


def weight_columns(out_weight, index, begin, width):
    block = out_weight.shape[0]
    return lax.dynamic_slice_in_dim(out_weight, index * block + begin, width, axis=1)


def ring_gather_dot(out_weight, out_grad, axis):
    count = lax.axis_size(axis)
    me = lax.axis_index(axis)
    block = out_grad.shape[0]
    half = block // 2

    def term(index, begin, width, piece):
        return jnp.dot(
            weight_columns(out_weight, index % count, begin, width),
            piece,
            preferred_element_type=jnp.float32,
        )

    total = term(me, 0, block, out_grad)
    ahead, behind = out_grad, out_grad
    for step in range(1, count // 2 + 1):
        if step < count - step:
            ahead = ring_shift(ahead, axis, 1)
            behind = ring_shift(behind, axis, -1)
            total = total + term(me - step, 0, block, ahead)
            total = total + term(me + step, 0, block, behind)
        else:
            low = ring_shift(ahead[:half], axis, 1)
            high = ring_shift(behind[half:], axis, -1)
            total = total + term(me - step, 0, half, low)
            total = total + term(me - step, half, half, high)
    return total


def per_device(queries, keys, values, out_weight, out_grad, doc_lengths):
    tok_rows = queries.shape[0]
    head_dim = keys.shape[1]
    group_size = queries.shape[1] // head_dim
    scaling = 1.0 / math.sqrt(head_dim)
    shard = lax.axis_index("ctx")
    doc_ends = jnp.cumsum(doc_lengths)
    starts = doc_ends - doc_lengths
    positions = shard * tok_rows + jnp.arange(tok_rows, dtype=jnp.int32)
    first_key = jnp.max(
        jnp.where(starts[None, :] <= positions[:, None], starts[None, :], 0), axis=1
    )
    stacked = jnp.concatenate([keys, values], axis=1)
    window = stacked[None]
    while 2 * window.shape[0] < REACH + 1:
        window = jnp.concatenate([window, passed_along(window, "ctx", window.shape[0])], axis=0)
    reach = window.shape[0]
    key_window = window[:, :, :head_dim]
    value_window = window[:, :, head_dim:]
    key_window = jnp.concatenate([key_window, passed_along(key_window, "ctx", reach)], axis=0)
    value_sent = passed_along(value_window, "ctx", reach)
    num_blocks = key_window.shape[0]
    flat_keys = key_window.reshape(num_blocks * tok_rows, head_dim)
    key_pos = (
        (shard - jnp.arange(num_blocks, dtype=jnp.int32))[:, None] * tok_rows
        + jnp.arange(tok_rows, dtype=jnp.int32)[None, :]
    ).reshape(-1)
    visible = (key_pos[None, :] >= first_key[:, None]) & (key_pos[None, :] <= positions[:, None])
    query_heads = queries.reshape(tok_rows, group_size, head_dim)
    scores = (
        jnp.einsum("tgd,kd->gtk", query_heads, flat_keys, preferred_element_type=jnp.float32)
        * scaling
    )
    scores = jnp.where(visible[None], scores, -jnp.inf)
    largest = jnp.max(scores, axis=-1, keepdims=True)
    expons = jnp.exp(scores - largest)
    weights = expons / jnp.sum(expons, axis=-1, keepdims=True)
    value_sent, weights = lax.optimization_barrier((value_sent, weights))
    value_window = jnp.concatenate([value_window, value_sent], axis=0)
    flat_values = value_window.reshape(num_blocks * tok_rows, head_dim)
    probs = weights.astype(jnp.bfloat16)
    attn_heads = jnp.einsum(
        "gtk,kd->tgd", probs, flat_values, preferred_element_type=jnp.float32
    ).astype(jnp.bfloat16)
    attn = attn_heads.reshape(tok_rows, group_size * head_dim)
    out_partial = lax.dot_general(
        out_weight, attn, (((0,), (1,)), ((), ())), preferred_element_type=jnp.float32
    ).astype(jnp.bfloat16)
    out_partial = with_layout_constraint(out_partial, Layout((0, 1)))
    out_t = lax.psum_scatter(
        out_partial, "heads", scatter_dimension=0, tiled=True
    )
    grad_attn = ring_gather_dot(out_weight, out_grad, "heads").astype(jnp.bfloat16)
    grad_heads = grad_attn.reshape(group_size, head_dim, tok_rows)
    delta_sum = jnp.einsum(
        "tgd,gdt->gt", attn_heads, grad_heads, preferred_element_type=jnp.float32
    )
    grad_probs = jnp.einsum(
        "gdt,kd->gtk", grad_heads, flat_values, preferred_element_type=jnp.float32
    )
    dscore = (weights * (grad_probs - delta_sum[:, :, None]) * scaling).astype(jnp.bfloat16)
    grad_q = (
        jnp.einsum("gtk,kd->tgd", dscore, flat_keys, preferred_element_type=jnp.float32)
        .astype(jnp.bfloat16)
        .reshape(tok_rows, group_size * head_dim)
    )
    key_part = jnp.einsum("gtk,tgd->kd", dscore, query_heads, preferred_element_type=jnp.float32)
    value_part = jnp.einsum("gtk,gdt->kd", probs, grad_heads, preferred_element_type=jnp.float32)
    partial_grads = jnp.concatenate([key_part, value_part], axis=1).reshape(
        num_blocks, tok_rows, 2 * head_dim
    )
    summed = partial_grads[0]
    for offset in range(1, num_blocks):
        sent = passed_along(partial_grads[offset].astype(jnp.bfloat16), "ctx", -offset)
        summed = summed + sent.astype(jnp.float32)
    grad_k = summed[:, :head_dim].astype(jnp.bfloat16)
    grad_v = summed[:, head_dim:].astype(jnp.bfloat16)
    return (out_t, grad_q, grad_k, grad_v)


def solution(mesh):
    placed = (
        P("ctx", "heads"),
        P("ctx", "heads"),
        P("ctx", "heads"),
        P("heads", None),
        P("heads", "ctx"),
        P(),
    )
    return jax.shard_map(
        per_device,
        mesh=mesh,
        in_specs=placed,
        out_specs=(P("heads", "ctx"), P("ctx", "heads"), P("ctx", "heads"), P("ctx", "heads")),
        check_vma=False,
    )
```

```python
import math

import jax
import jax.numpy as jnp
from jax import lax
from jax.experimental.layout import Layout, with_layout_constraint
from jax.sharding import PartitionSpec as P

REACH = 7


def passed_along(value, axis, steps):
    count = lax.axis_size(axis)
    first, last = (max(0, -steps), min(count, count - steps))
    return lax.ppermute(value, axis, [(source, source + steps) for source in range(first, last)])


def softmax_weights(query_heads, flat_keys, visible, scaling):
    scores = (
        jnp.einsum("tgd,kd->gtk", query_heads, flat_keys, preferred_element_type=jnp.float32)
        * scaling
    )
    scores = jnp.where(visible[None], scores, -jnp.inf)
    largest = jnp.max(scores, axis=-1, keepdims=True)
    expons = jnp.exp(scores - largest)
    return expons / jnp.sum(expons, axis=-1, keepdims=True)


def per_device(queries, keys, values, out_weight, out_grad, doc_lengths):
    tok_rows = queries.shape[0]
    head_dim = keys.shape[1]
    group_size = queries.shape[1] // head_dim
    scaling = 1.0 / math.sqrt(head_dim)
    shard = lax.axis_index("ctx")
    doc_ends = jnp.cumsum(doc_lengths)
    starts = doc_ends - doc_lengths
    positions = shard * tok_rows + jnp.arange(tok_rows, dtype=jnp.int32)
    first_key = jnp.max(
        jnp.where(starts[None, :] <= positions[:, None], starts[None, :], 0), axis=1
    )
    stacked = jnp.concatenate([keys, values], axis=1)
    window = stacked[None]
    while 2 * window.shape[0] < REACH + 1:
        window = jnp.concatenate([window, passed_along(window, "ctx", window.shape[0])], axis=0)
    reach = window.shape[0]
    key_window = window[:, :, :head_dim]
    value_window = window[:, :, head_dim:]
    key_window = jnp.concatenate([key_window, passed_along(key_window, "ctx", reach)], axis=0)
    value_sent = passed_along(value_window, "ctx", reach)
    num_blocks = key_window.shape[0]
    flat_keys = key_window.reshape(num_blocks * tok_rows, head_dim)
    key_pos = (
        (shard - jnp.arange(num_blocks, dtype=jnp.int32))[:, None] * tok_rows
        + jnp.arange(tok_rows, dtype=jnp.int32)[None, :]
    ).reshape(-1)
    visible = (key_pos[None, :] >= first_key[:, None]) & (key_pos[None, :] <= positions[:, None])
    query_heads = queries.reshape(tok_rows, group_size, head_dim)
    weights = softmax_weights(query_heads, flat_keys, visible, scaling)
    probs = weights.astype(jnp.bfloat16)
    value_sent, probs = lax.optimization_barrier((value_sent, probs))
    value_window = jnp.concatenate([value_window, value_sent], axis=0)
    flat_values = value_window.reshape(num_blocks * tok_rows, head_dim)
    attn_heads = jnp.einsum(
        "gtk,kd->tgd", probs, flat_values, preferred_element_type=jnp.float32
    ).astype(jnp.bfloat16)
    attn = attn_heads.reshape(tok_rows, group_size * head_dim)
    out_partial = lax.dot_general(
        out_weight, attn, (((0,), (1,)), ((), ())), preferred_element_type=jnp.float32
    ).astype(jnp.bfloat16)
    out_partial = with_layout_constraint(out_partial, Layout((0, 1)))
    gathered = lax.all_gather(out_grad, "heads", axis=0, tiled=True)
    out_t = lax.psum_scatter(
        out_partial, "heads", scatter_dimension=0, tiled=True
    )
    _, gathered, query_again, keys_again = lax.optimization_barrier(
        (out_partial, gathered, query_heads, flat_keys)
    )
    weights = softmax_weights(query_again, keys_again, visible, scaling)
    grad_attn = jnp.dot(
        out_weight,
        gathered,
        preferred_element_type=jnp.float32,
    ).astype(jnp.bfloat16)
    grad_heads = grad_attn.reshape(group_size, head_dim, tok_rows)
    delta_sum = jnp.einsum(
        "tgd,gdt->gt", attn_heads, grad_heads, preferred_element_type=jnp.float32
    )
    grad_probs = jnp.einsum(
        "gdt,kd->gtk", grad_heads, flat_values, preferred_element_type=jnp.float32
    )
    dscore = (weights * (grad_probs - delta_sum[:, :, None]) * scaling).astype(jnp.bfloat16)
    grad_q = (
        jnp.einsum("gtk,kd->tgd", dscore, flat_keys, preferred_element_type=jnp.float32)
        .astype(jnp.bfloat16)
        .reshape(tok_rows, group_size * head_dim)
    )
    key_part = jnp.einsum("gtk,tgd->kd", dscore, query_heads, preferred_element_type=jnp.float32)
    value_part = jnp.einsum("gtk,gdt->kd", probs, grad_heads, preferred_element_type=jnp.float32)
    partial_grads = jnp.concatenate([key_part, value_part], axis=1).reshape(
        num_blocks, tok_rows, 2 * head_dim
    )
    summed = partial_grads[0]
    for offset in range(1, num_blocks):
        sent = passed_along(partial_grads[offset].astype(jnp.bfloat16), "ctx", -offset)
        summed = summed + sent.astype(jnp.float32)
    grad_k = summed[:, :head_dim].astype(jnp.bfloat16)
    grad_v = summed[:, head_dim:].astype(jnp.bfloat16)
    return (out_t, grad_q, grad_k, grad_v)


def solution(mesh):
    placed = (
        P("ctx", "heads"),
        P("ctx", "heads"),
        P("ctx", "heads"),
        P("heads", None),
        P("heads", "ctx"),
        P(),
    )
    return jax.shard_map(
        per_device,
        mesh=mesh,
        in_specs=placed,
        out_specs=(P("heads", "ctx"), P("ctx", "heads"), P("ctx", "heads"), P("ctx", "heads")),
        check_vma=False,
    )
```

```python
import math

import jax
import jax.numpy as jnp
from jax import lax
from jax.experimental.layout import Layout, with_layout_constraint
from jax.sharding import PartitionSpec as P

REACH = 7


def passed_along(value, axis, steps):
    count = lax.axis_size(axis)
    first, last = (max(0, -steps), min(count, count - steps))
    return lax.ppermute(value, axis, [(source, source + steps) for source in range(first, last)])


def per_device(queries, keys, values, out_weight, out_grad, doc_lengths):
    tok_rows = queries.shape[0]
    head_dim = keys.shape[1]
    group_size = queries.shape[1] // head_dim
    scaling = 1.0 / math.sqrt(head_dim)
    shard = lax.axis_index("ctx")
    doc_ends = jnp.cumsum(doc_lengths)
    starts = doc_ends - doc_lengths
    positions = shard * tok_rows + jnp.arange(tok_rows, dtype=jnp.int32)
    first_key = jnp.max(
        jnp.where(starts[None, :] <= positions[:, None], starts[None, :], 0), axis=1
    )
    stacked = jnp.concatenate([keys, values], axis=1)
    window = stacked[None]
    while 2 * window.shape[0] < REACH + 1:
        window = jnp.concatenate([window, passed_along(window, "ctx", window.shape[0])], axis=0)
    reach = window.shape[0]
    key_window = window[:, :, :head_dim]
    value_window = window[:, :, head_dim:]
    key_window = jnp.concatenate([key_window, passed_along(key_window, "ctx", reach)], axis=0)
    value_sent = passed_along(value_window, "ctx", reach)
    num_blocks = key_window.shape[0]
    flat_keys = key_window.reshape(num_blocks * tok_rows, head_dim)
    key_pos = (
        (shard - jnp.arange(num_blocks, dtype=jnp.int32))[:, None] * tok_rows
        + jnp.arange(tok_rows, dtype=jnp.int32)[None, :]
    ).reshape(-1)
    visible = (key_pos[None, :] >= first_key[:, None]) & (key_pos[None, :] <= positions[:, None])
    query_heads = queries.reshape(tok_rows, group_size, head_dim)
    scores = (
        jnp.einsum("tgd,kd->gtk", query_heads, flat_keys, preferred_element_type=jnp.float32)
        * scaling
    )
    scores = jnp.where(visible[None], scores, -jnp.inf)
    largest = jnp.max(scores, axis=-1, keepdims=True)
    expons = jnp.exp(scores - largest)
    weights = expons / jnp.sum(expons, axis=-1, keepdims=True)
    probs = weights.astype(jnp.bfloat16)
    value_sent, probs = lax.optimization_barrier((value_sent, probs))
    value_window = jnp.concatenate([value_window, value_sent], axis=0)
    flat_values = value_window.reshape(num_blocks * tok_rows, head_dim)
    attn_heads = jnp.einsum(
        "gtk,kd->tgd", probs, flat_values, preferred_element_type=jnp.float32
    ).astype(jnp.bfloat16)
    attn = attn_heads.reshape(tok_rows, group_size * head_dim)
    out_partial = lax.dot_general(
        out_weight, attn, (((0,), (1,)), ((), ())), preferred_element_type=jnp.float32
    ).astype(jnp.bfloat16)
    out_partial = with_layout_constraint(out_partial, Layout((0, 1)))
    gathered = lax.all_gather(out_grad, "heads", axis=0, tiled=True)
    out_t = lax.psum_scatter(
        out_partial, "heads", scatter_dimension=0, tiled=True
    )
    _, gathered = lax.optimization_barrier((out_partial, gathered))
    grad_attn = jnp.dot(
        out_weight,
        gathered,
        preferred_element_type=jnp.float32,
    ).astype(jnp.bfloat16)
    grad_heads = grad_attn.reshape(group_size, head_dim, tok_rows)
    delta_sum = jnp.einsum(
        "tgd,gdt->gt", attn_heads, grad_heads, preferred_element_type=jnp.float32
    )
    grad_probs = jnp.einsum(
        "gdt,kd->gtk", grad_heads, flat_values, preferred_element_type=jnp.float32
    )
    dscore = (weights * (grad_probs - delta_sum[:, :, None]) * scaling).astype(jnp.bfloat16)
    grad_q = (
        jnp.einsum("gtk,kd->tgd", dscore, flat_keys, preferred_element_type=jnp.float32)
        .astype(jnp.bfloat16)
        .reshape(tok_rows, group_size * head_dim)
    )
    key_part = jnp.einsum("gtk,tgd->kd", dscore, query_heads, preferred_element_type=jnp.float32)
    value_part = jnp.einsum("gtk,gdt->kd", probs, grad_heads, preferred_element_type=jnp.float32)
    partial_grads = jnp.concatenate([key_part, value_part], axis=1).reshape(
        num_blocks, tok_rows, 2 * head_dim
    )
    summed = partial_grads[0]
    for offset in range(1, num_blocks):
        sent = passed_along(partial_grads[offset].astype(jnp.bfloat16), "ctx", -offset)
        summed = summed + sent.astype(jnp.float32)
    grad_k = summed[:, :head_dim].astype(jnp.bfloat16)
    grad_v = summed[:, head_dim:].astype(jnp.bfloat16)
    return (out_t, grad_q, grad_k, grad_v)


def solution(mesh):
    placed = (
        P("ctx", "heads"),
        P("ctx", "heads"),
        P("ctx", "heads"),
        P("heads", None),
        P("heads", "ctx"),
        P(),
    )
    return jax.shard_map(
        per_device,
        mesh=mesh,
        in_specs=placed,
        out_specs=(P("heads", "ctx"), P("ctx", "heads"), P("ctx", "heads"), P("ctx", "heads")),
        check_vma=False,
    )
```
